256 devices in a mesh: layer: 64 (over z, x, y_lo), dp: 4 (over y_hi, core).
Axes of the slice: x: 4, y: 4 (y_hi: 2, y_lo: 2; y = y_hi * 2 + y_lo), z: 8, core: 2. Of those that a mesh axis runs over, the one named last changes fastest.
Arguments:
- inputs: bfloat16 [512, 2048], P('dp'), may hold values from -6 to 6
- weights: bfloat16 [64, 2048, 2048], P('layer'), may hold values from -0.125 to 0.125
- precision: float32 [64], P('layer'), may hold values from 0.8 to 7.5, as said below
- activity: float32 [64, 512, 2048], P('layer', 'dp'), may hold values from -5 to 5
Outputs:
- relaxed: float32 [64, 512, 2048], P('layer', 'dp')
- update: bfloat16 [64, 2048, 2048], P('layer', 'dp')
The draws below stay inside these ranges and needn't reach their ends.
Inputs may be any that keep to these rules, and one draw needn't show every extreme that they name: `precision`: positive weights of the layers' errors.
All inputs are finite; a program needn't handle non-finite values.
Results may differ from the reference program's by a relative error of at most 0.02.
Values may be sent and summed in bfloat16 or wider, within the bound.
No kernel may reach another device: no remote copies, remote signals or barrier semaphores. Data moves between devices by JAX's collectives and lax.ppermute only.
A program may use at most 64 MiB of HBM per device.

```python
import jax
import jax.numpy as jnp
from jax import lax

D = 2048
ROWS_DEV = 128
ITERS = 5
LAYERS = 64
BATCH = 512


def draw_precision(key, part):
    position = jnp.arange(LAYERS).astype(jnp.float32) / max(LAYERS - 1, 1)
    base_level = 1.0 + 2.0 * position
    factor = jax.random.uniform(key, (LAYERS,), jnp.float32, 0.8, 1.25)
    return (base_level * factor).astype(jnp.float32)


def draw_activity(key, part):
    noise_key = jax.random.fold_in(key, 11)
    common_key = jax.random.fold_in(key, 23)
    block_count = BATCH // ROWS_DEV
    noise = jax.random.normal(noise_key, (LAYERS, BATCH, D), jnp.float32)
    amplitude = 0.4
    common = jax.random.normal(common_key, (LAYERS, block_count, 1, D), jnp.float32)
    common = jnp.broadcast_to(common, (LAYERS, block_count, ROWS_DEV, D)).reshape(LAYERS, BATCH, D)
    return jnp.clip(noise + amplitude * common, -5.0, 5.0).astype(jnp.float32)


def shard_levels(rng, shape, shards, least, high):
    level = 1.0
    for dim, blocks in shards:
        heights = jax.random.uniform(jax.random.fold_in(jax.random.fold_in(rng, 6), dim), (blocks,), jnp.float32, least / len(shards), high / len(shards))
        level = level * jnp.repeat(jnp.exp(heights), shape[dim] // blocks).reshape((-1,) + (1,) * (len(shape) - 1 - dim))
    return level


def gaussian(key, extent, spread, reach, shards=(), held_as=jnp.bfloat16):
    level = shard_levels(key, extent, shards, -0.22, 0.18) if shards else 1.0
    array = jax.random.normal(key, extent, jnp.float32) * spread * level
    return jnp.minimum(jnp.maximum(array, -reach), reach).astype(held_as)


def setup_inputs(seed: int = 0) -> dict:
    streams_of = jax.random.split(jax.random.key(seed), 5)
    inputs = gaussian(streams_of[0], (BATCH, D), 1.0, 6.0, ((0, 4),))
    weights = gaussian(streams_of[1], (LAYERS, D, D), D ** -0.5, 0.125, ((0, 64),))
    precision = draw_precision(jax.random.fold_in(streams_of[4], 71), 0)
    activity = draw_activity(jax.random.fold_in(streams_of[4], 71), 0)
    return dict(inputs=inputs, weights=weights, precision=precision, activity=activity)


step_rate = 0.1

def reference(inputs, weights, precision, activity):
    bottom_input = jnp.tanh(inputs.astype(jnp.float32)).astype(jnp.bfloat16)
    weighting = precision[:, None, None]
    clamped = (jnp.arange(LAYERS) == LAYERS - 1)[:, None, None]

    def predict(state):
        squashed = jnp.tanh(state)
        lower_input = jnp.concatenate([bottom_input[None], squashed[:-1].astype(jnp.bfloat16)], 0)
        predicted = lax.map(lambda pair: jnp.dot(pair[0], pair[1], preferred_element_type=jnp.float32), (lower_input, weights))
        mismatch = state - predicted
        weighted = (weighting * mismatch).astype(jnp.bfloat16)
        return (squashed, lower_input, mismatch, weighted)
    state = activity
    for _ in range(ITERS):
        squashed, lower_input, mismatch, weighted = predict(state)
        downward = lax.map(lambda pair: jnp.dot(pair[0], pair[1].T, preferred_element_type=jnp.float32), (weighted, weights)).astype(jnp.bfloat16)
        from_above = jnp.concatenate([downward[1:], jnp.zeros_like(downward[:1])], 0).astype(jnp.float32)
        descent = weighting * mismatch - (1.0 - squashed * squashed) * from_above
        state = jnp.where(clamped, state, state - step_rate * descent)
    squashed, lower_input, mismatch, weighted = predict(state)
    gradient = lax.map(lambda pair: jnp.dot(pair[0].T, pair[1], preferred_element_type=jnp.float32), (lower_input, weighted))
    square_total = jnp.sum(gradient * gradient)
    root_mean = jnp.sqrt(square_total / (LAYERS * D * D) + 1e-06)
    clip_factor = jnp.minimum(1.0, 1.0 / root_mean)
    return (state, (gradient * clip_factor).astype(jnp.bfloat16))
```

```python
import jax
import jax.numpy as jnp
from jax import lax
from jax.sharding import PartitionSpec as P

ITERS = 5


step_rate = 0.1


def shifted(x, axis, by):
    length = lax.axis_size(axis)
    pairs = [(i, i + by) for i in range(length) if 0 <= i + by < length]
    return lax.ppermute(x, axis, pairs)


def row_exchange_gradient(lower_input, weighted):
    count = lax.axis_size("dp")
    index = lax.axis_index("dp")
    block = lower_input.shape[1] // count

    def columns(owner):
        return lax.dynamic_slice_in_dim(lower_input, owner * block, block, 1)

    total = jnp.einsum("rc,re->ce", columns(index), weighted, preferred_element_type=jnp.float32)
    for by in range(1, count):
        pairs = [(j, (j + by) % count) for j in range(count)]
        their_columns = lax.ppermute(columns((index + by) % count), "dp", pairs)
        their_weighted = lax.ppermute(weighted, "dp", pairs)
        total = total + jnp.einsum(
            "rc,re->ce", their_columns, their_weighted, preferred_element_type=jnp.float32
        )
    return total


def group_sum(value, axis, size, stride):
    length = lax.axis_size(axis)
    index = lax.axis_index(axis)
    digit = (index // stride) % size
    slots = jnp.zeros((size,), value.dtype).at[digit].set(value)
    for by in range(1, size):
        pairs = []
        for i in range(length):
            d = (i // stride) % size
            pairs.append((i, i + (((d + by) % size) - d) * stride))
        arrived = lax.ppermute(value, axis, pairs)
        slots = slots.at[(digit - by) % size].set(arrived)
    return jnp.sum(slots)


def group_total(value):
    value = group_sum(value, "dp", lax.axis_size("dp"), 1)
    length = lax.axis_size("layer")
    stride = 1
    while stride < length:
        size = min(8, length // stride)
        value = group_sum(value, "layer", size, stride)
        stride *= size
    return value


def shards(inputs, weights, precision, activity):
    layer_count = lax.axis_size("layer")
    position = lax.axis_index("layer")
    local_layers = weights.shape[0]
    width = weights.shape[1]
    bottom_input = jnp.tanh(inputs.astype(jnp.float32)).astype(jnp.bfloat16)
    weighting = precision[:, None, None]
    global_layer = position * local_layers + jnp.arange(local_layers)
    clamped = (global_layer == local_layers * layer_count - 1)[:, None, None]

    def predict(state):
        squashed = jnp.tanh(state)
        squashed_low = squashed.astype(jnp.bfloat16)
        arriving = shifted(squashed_low[-1], "layer", 1)
        arriving = jnp.where(position == 0, bottom_input, arriving)
        lower_input = jnp.concatenate([arriving[None], squashed_low[:-1]], 0)
        predicted = jnp.einsum(
            "lrd,lde->lre", lower_input, weights, preferred_element_type=jnp.float32
        )
        mismatch = state - predicted
        weighted = (weighting * mismatch).astype(jnp.bfloat16)
        return (squashed, lower_input, mismatch, weighted)

    state = activity
    for _ in range(ITERS):
        squashed, lower_input, mismatch, weighted = predict(state)
        downward = jnp.einsum(
            "lre,lde->lrd", weighted, weights, preferred_element_type=jnp.float32
        ).astype(jnp.bfloat16)
        incoming = shifted(downward[0], "layer", -1)
        from_above = jnp.concatenate([downward[1:], incoming[None]], 0).astype(jnp.float32)
        descent = weighting * mismatch - (1.0 - squashed * squashed) * from_above
        state = jnp.where(clamped, state, state - step_rate * descent)
    squashed, lower_input, mismatch, weighted = predict(state)
    gradient = row_exchange_gradient(lower_input[0], weighted[0])[None]
    square_total = group_total(jnp.sum(gradient * gradient))
    entry_count = float(local_layers * layer_count * width * width)
    root_mean = jnp.sqrt(square_total / entry_count + 1e-06)
    clip_factor = jnp.minimum(1.0, 1.0 / root_mean)
    return (state, (gradient * clip_factor).astype(jnp.bfloat16))


def solution(mesh):
    in_specs = (P("dp", None), P("layer", None, None), P("layer"), P("layer", "dp", None))
    out_specs = (P("layer", "dp", None), P("layer", "dp", None))
    return jax.shard_map(shards, mesh=mesh, in_specs=in_specs, out_specs=out_specs, check_vma=False)
```

```python
import jax
import jax.numpy as jnp
from jax import lax
from jax.sharding import PartitionSpec as P

ITERS = 5
CHUNKS = 2


step_rate = 0.1


def shifted(x, axis, by):
    length = lax.axis_size(axis)
    pairs = [(i, i + by) for i in range(length) if 0 <= i + by < length]
    return lax.ppermute(x, axis, pairs)


def row_exchange_gradient(lower_input, weighted):
    count = lax.axis_size("dp")
    index = lax.axis_index("dp")
    block = lower_input.shape[1] // count

    def columns(owner):
        return lax.dynamic_slice_in_dim(lower_input, owner * block, block, 1)

    total = jnp.einsum("rc,re->ce", columns(index), weighted, preferred_element_type=jnp.float32)
    for by in range(1, count):
        pairs = [(j, (j + by) % count) for j in range(count)]
        their_columns = lax.ppermute(columns((index + by) % count), "dp", pairs)
        their_weighted = lax.ppermute(weighted, "dp", pairs)
        total = total + jnp.einsum(
            "rc,re->ce", their_columns, their_weighted, preferred_element_type=jnp.float32
        )
    return total


def global_total(value):
    axes = ("layer", "dp")
    count = lax.axis_size("layer") * lax.axis_size("dp")
    spread = jnp.broadcast_to(value, (count, 1))
    gathered = lax.all_to_all(spread, axes, 0, 0, tiled=True)
    return jnp.sum(gathered)


def shards(inputs, weights, precision, activity):
    layer_count = lax.axis_size("layer")
    position = lax.axis_index("layer")
    local_layers = weights.shape[0]
    assert local_layers == 1
    width = weights.shape[1]
    weight = weights[0]
    weighting = precision[0]
    bottom_input = jnp.tanh(inputs.astype(jnp.float32)).astype(jnp.bfloat16)
    clamped = position == layer_count - 1
    rows = activity.shape[1]
    size = rows // CHUNKS
    states = [activity[0, c * size:(c + 1) * size] for c in range(CHUNKS)]
    bottoms = [bottom_input[c * size:(c + 1) * size] for c in range(CHUNKS)]

    def lower_inputs(states):
        squashed = [jnp.tanh(s) for s in states]
        arriving = [shifted(q.astype(jnp.bfloat16), "layer", 1) for q in squashed]
        lowers = [jnp.where(position == 0, b, a) for b, a in zip(bottoms, arriving)]
        return squashed, lowers

    def errors(state, lower):
        predicted = jnp.dot(lower, weight, preferred_element_type=jnp.float32)
        mismatch = state - predicted
        weighted = (weighting * mismatch).astype(jnp.bfloat16)
        return mismatch, weighted

    for _ in range(ITERS):
        squashed, lowers = lower_inputs(states)
        new_states = []
        for state, q, lower in zip(states, squashed, lowers):
            mismatch, weighted = errors(state, lower)
            downward = lax.dot_general(
                weighted, weight, (((1,), (1,)), ((), ())), preferred_element_type=jnp.float32
            ).astype(jnp.bfloat16)
            from_above = shifted(downward, "layer", -1).astype(jnp.float32)
            descent = weighting * mismatch - (1.0 - q * q) * from_above
            new_states.append(jnp.where(clamped, state, state - step_rate * descent))
        states = new_states
    squashed, lowers = lower_inputs(states)
    weighteds = [errors(s, l)[1] for s, l in zip(states, lowers)]
    lower_input = jnp.concatenate(lowers, 0)
    weighted = jnp.concatenate(weighteds, 0)
    gradient = row_exchange_gradient(lower_input, weighted)[None]
    square_total = global_total(jnp.sum(gradient * gradient))
    entry_count = float(local_layers * layer_count * width * width)
    root_mean = jnp.sqrt(square_total / entry_count + 1e-06)
    clip_factor = jnp.minimum(1.0, 1.0 / root_mean)
    relaxed = jnp.concatenate(states, 0)[None]
    return (relaxed, (gradient * clip_factor).astype(jnp.bfloat16))


def solution(mesh):
    in_specs = (P("dp", None), P("layer", None, None), P("layer"), P("layer", "dp", None))
    out_specs = (P("layer", "dp", None), P("layer", "dp", None))
    return jax.shard_map(shards, mesh=mesh, in_specs=in_specs, out_specs=out_specs, check_vma=False)
```

```python
import jax
import jax.numpy as jnp
from jax import lax
from jax.sharding import PartitionSpec as P

ITERS = 5
CHUNKS = 4


step_rate = 0.1


def shifted(x, axis, by):
    length = lax.axis_size(axis)
    pairs = [(i, i + by) for i in range(length) if 0 <= i + by < length]
    return lax.ppermute(x, axis, pairs)


def row_exchange_gradient(lower_input, weighted):
    count = lax.axis_size("dp")
    index = lax.axis_index("dp")
    block = lower_input.shape[1] // count

    def columns(owner):
        return lax.dynamic_slice_in_dim(lower_input, owner * block, block, 1)

    total = jnp.einsum("rc,re->ce", columns(index), weighted, preferred_element_type=jnp.float32)
    for by in range(1, count):
        pairs = [(j, (j + by) % count) for j in range(count)]
        their_columns = lax.ppermute(columns((index + by) % count), "dp", pairs)
        their_weighted = lax.ppermute(weighted, "dp", pairs)
        total = total + jnp.einsum(
            "rc,re->ce", their_columns, their_weighted, preferred_element_type=jnp.float32
        )
    return total


def global_total(value):
    axes = ("layer", "dp")
    count = lax.axis_size("layer") * lax.axis_size("dp")
    spread = jnp.broadcast_to(value, (count, 1))
    gathered = lax.all_to_all(spread, axes, 0, 0, tiled=True)
    return jnp.sum(gathered)


def shards(inputs, weights, precision, activity):
    layer_count = lax.axis_size("layer")
    position = lax.axis_index("layer")
    local_layers = weights.shape[0]
    assert local_layers == 1
    width = weights.shape[1]
    weight = weights[0]
    weighting = precision[0]
    bottom_input = jnp.tanh(inputs.astype(jnp.float32)).astype(jnp.bfloat16)
    clamped = position == layer_count - 1
    rows = activity.shape[1]
    size = rows // CHUNKS
    states = [activity[0, c * size:(c + 1) * size] for c in range(CHUNKS)]
    bottoms = [bottom_input[c * size:(c + 1) * size] for c in range(CHUNKS)]

    def lower_inputs(states):
        squashed = [jnp.tanh(s) for s in states]
        arriving = [shifted(q.astype(jnp.bfloat16), "layer", 1) for q in squashed]
        lowers = [jnp.where(position == 0, b, a) for b, a in zip(bottoms, arriving)]
        return squashed, lowers

    def errors(state, lower):
        predicted = jnp.dot(lower, weight, preferred_element_type=jnp.float32)
        mismatch = state - predicted
        weighted = (weighting * mismatch).astype(jnp.bfloat16)
        return mismatch, weighted

    for _ in range(ITERS):
        squashed, lowers = lower_inputs(states)
        new_states = []
        for state, q, lower in zip(states, squashed, lowers):
            mismatch, weighted = errors(state, lower)
            downward = lax.dot_general(
                weighted, weight, (((1,), (1,)), ((), ())), preferred_element_type=jnp.float32
            ).astype(jnp.bfloat16)
            from_above = shifted(downward, "layer", -1).astype(jnp.float32)
            descent = weighting * mismatch - (1.0 - q * q) * from_above
            new_states.append(jnp.where(clamped, state, state - step_rate * descent))
        states = new_states
    squashed, lowers = lower_inputs(states)
    weighteds = [errors(s, l)[1] for s, l in zip(states, lowers)]
    lower_input = jnp.concatenate(lowers, 0)
    weighted = jnp.concatenate(weighteds, 0)
    gradient = row_exchange_gradient(lower_input, weighted)[None]
    square_total = global_total(jnp.sum(gradient * gradient))
    entry_count = float(local_layers * layer_count * width * width)
    root_mean = jnp.sqrt(square_total / entry_count + 1e-06)
    clip_factor = jnp.minimum(1.0, 1.0 / root_mean)
    relaxed = jnp.concatenate(states, 0)[None]
    return (relaxed, (gradient * clip_factor).astype(jnp.bfloat16))


def solution(mesh):
    in_specs = (P("dp", None), P("layer", None, None), P("layer"), P("layer", "dp", None))
    out_specs = (P("layer", "dp", None), P("layer", "dp", None))
    return jax.shard_map(shards, mesh=mesh, in_specs=in_specs, out_specs=out_specs, check_vma=False)
```

```python
import jax
import jax.numpy as jnp
from jax import lax
from jax.sharding import PartitionSpec as P

ITERS = 5
CHUNKS = 2


step_rate = 0.1


def shifted(x, axis, by):
    length = lax.axis_size(axis)
    pairs = [(i, i + by) for i in range(length) if 0 <= i + by < length]
    return lax.ppermute(x, axis, pairs)


def row_exchange_gradient(lower_input, weighted):
    count = lax.axis_size("dp")
    index = lax.axis_index("dp")
    assert count == 4
    block = lower_input.shape[1] // count
    core = index % 2
    other_chip = 1 - index // 2

    def cols(a, start, size):
        return lax.dynamic_slice_in_dim(a, start, size, 1)

    across = jnp.concatenate([weighted, cols(lower_input, other_chip * 2 * block, 2 * block)], 1)
    arrived = lax.ppermute(across, "dp", [(j, j ^ 2) for j in range(count)])
    far_weighted = arrived[:, : weighted.shape[1]]
    far_columns = arrived[:, weighted.shape[1]:]
    partner = 1 - core
    beside = jnp.concatenate(
        [
            jnp.concatenate([weighted, cols(lower_input, (index ^ 1) * block, block)], 1),
            jnp.concatenate([far_weighted, cols(far_columns, partner * block, block)], 1),
        ],
        0,
    )
    near = lax.ppermute(beside, "dp", [(j, j ^ 1) for j in range(count)])
    own_rows = jnp.concatenate([cols(lower_input, index * block, block), cols(far_columns, core * block, block)], 0)
    own_weighted = jnp.concatenate([weighted, far_weighted], 0)
    total = jnp.einsum("rc,re->ce", own_rows, own_weighted, preferred_element_type=jnp.float32)
    total = total + jnp.einsum(
        "rc,re->ce", near[:, weighted.shape[1]:], near[:, : weighted.shape[1]], preferred_element_type=jnp.float32
    )
    return total


def global_total(value):
    axes = ("layer", "dp")
    count = lax.axis_size("layer") * lax.axis_size("dp")
    spread = jnp.broadcast_to(value, (count, 1))
    gathered = lax.all_to_all(spread, axes, 0, 0, tiled=True)
    return jnp.sum(gathered)


def shards(inputs, weights, precision, activity):
    layer_count = lax.axis_size("layer")
    position = lax.axis_index("layer")
    local_layers = weights.shape[0]
    assert local_layers == 1
    width = weights.shape[1]
    weight = weights[0]
    weighting = precision[0]
    bottom_input = jnp.tanh(inputs.astype(jnp.float32)).astype(jnp.bfloat16)
    clamped = position == layer_count - 1
    rows = activity.shape[1]
    size = rows // CHUNKS
    states = [activity[0, c * size:(c + 1) * size] for c in range(CHUNKS)]
    bottoms = [bottom_input[c * size:(c + 1) * size] for c in range(CHUNKS)]

    def lower_inputs(states):
        squashed = [jnp.tanh(s) for s in states]
        arriving = [shifted(q.astype(jnp.bfloat16), "layer", 1) for q in squashed]
        lowers = [jnp.where(position == 0, b, a) for b, a in zip(bottoms, arriving)]
        return squashed, lowers

    def errors(state, lower):
        predicted = jnp.dot(lower, weight, preferred_element_type=jnp.float32)
        mismatch = state - predicted
        weighted = (weighting * mismatch).astype(jnp.bfloat16)
        return mismatch, weighted

    for _ in range(ITERS):
        squashed, lowers = lower_inputs(states)
        new_states = []
        for state, q, lower in zip(states, squashed, lowers):
            mismatch, weighted = errors(state, lower)
            downward = lax.dot_general(
                weighted, weight, (((1,), (1,)), ((), ())), preferred_element_type=jnp.float32
            ).astype(jnp.bfloat16)
            from_above = shifted(downward, "layer", -1).astype(jnp.float32)
            descent = weighting * mismatch - (1.0 - q * q) * from_above
            new_states.append(jnp.where(clamped, state, state - step_rate * descent))
        states = new_states
    squashed, lowers = lower_inputs(states)
    weighteds = [errors(s, l)[1] for s, l in zip(states, lowers)]
    lower_input = jnp.concatenate(lowers, 0)
    weighted = jnp.concatenate(weighteds, 0)
    gradient = row_exchange_gradient(lower_input, weighted)[None]
    square_total = global_total(jnp.sum(gradient * gradient))
    entry_count = float(local_layers * layer_count * width * width)
    root_mean = jnp.sqrt(square_total / entry_count + 1e-06)
    clip_factor = jnp.minimum(1.0, 1.0 / root_mean)
    relaxed = jnp.concatenate(states, 0)[None]
    return (relaxed, (gradient * clip_factor).astype(jnp.bfloat16))


def solution(mesh):
    in_specs = (P("dp", None), P("layer", None, None), P("layer"), P("layer", "dp", None))
    out_specs = (P("layer", "dp", None), P("layer", "dp", None))
    return jax.shard_map(shards, mesh=mesh, in_specs=in_specs, out_specs=out_specs, check_vma=False)
```

```python
import jax
import jax.numpy as jnp
from jax import lax
from jax.sharding import PartitionSpec as P

ITERS = 5
CHUNKS = 2


step_rate = 0.1


def shifted(x, axis, by):
    length = lax.axis_size(axis)
    pairs = [(i, i + by) for i in range(length) if 0 <= i + by < length]
    return lax.ppermute(x, axis, pairs)


def row_exchange_gradient(lower_input, weighted):
    count = lax.axis_size("dp")
    index = lax.axis_index("dp")
    assert count == 4
    block = lower_input.shape[1] // count
    core = index % 2
    other_chip = 1 - index // 2

    def cols(a, start, size):
        return lax.dynamic_slice_in_dim(a, start, size, 1)

    across = jnp.concatenate([weighted, cols(lower_input, other_chip * 2 * block, 2 * block)], 1)
    arrived = lax.ppermute(across, "dp", [(j, j ^ 2) for j in range(count)])
    far_weighted = arrived[:, : weighted.shape[1]]
    far_columns = arrived[:, weighted.shape[1]:]
    partner = 1 - core
    beside = jnp.concatenate(
        [
            jnp.concatenate([weighted, cols(lower_input, (index ^ 1) * block, block)], 1),
            jnp.concatenate([far_weighted, cols(far_columns, partner * block, block)], 1),
        ],
        0,
    )
    near = lax.ppermute(beside, "dp", [(j, j ^ 1) for j in range(count)])
    own_rows = jnp.concatenate([cols(lower_input, index * block, block), cols(far_columns, core * block, block)], 0)
    own_weighted = jnp.concatenate([weighted, far_weighted], 0)
    total = jnp.einsum("rc,re->ce", own_rows, own_weighted, preferred_element_type=jnp.float32)
    total = total + jnp.einsum(
        "rc,re->ce", near[:, weighted.shape[1]:], near[:, : weighted.shape[1]], preferred_element_type=jnp.float32
    )
    return total


def global_total(value):
    axes = ("layer", "dp")
    count = lax.axis_size("layer") * lax.axis_size("dp")
    spread = jnp.broadcast_to(value, (count, 1))
    gathered = lax.all_to_all(spread, axes, 0, 0, tiled=True)
    return jnp.sum(gathered)


def shards(inputs, weights, precision, activity):
    layer_count = lax.axis_size("layer")
    position = lax.axis_index("layer")
    local_layers = weights.shape[0]
    assert local_layers == 1
    width = weights.shape[1]
    weight = weights[0]
    weighting = precision[0]
    bottom_input = jnp.tanh(inputs.astype(jnp.float32)).astype(jnp.bfloat16)
    clamped = position == layer_count - 1
    rows = activity.shape[1]
    size = rows // CHUNKS
    states = [activity[0, c * size:(c + 1) * size] for c in range(CHUNKS)]
    bottoms = [bottom_input[c * size:(c + 1) * size] for c in range(CHUNKS)]

    def lower_inputs(states):
        squashed = [jnp.tanh(s) for s in states]
        together = jnp.concatenate([q.astype(jnp.bfloat16) for q in squashed], 0)
        arriving = shifted(together, "layer", 1)
        arriving = [arriving[c * size:(c + 1) * size] for c in range(CHUNKS)]
        lowers = [jnp.where(position == 0, b, a) for b, a in zip(bottoms, arriving)]
        return squashed, lowers

    def errors(state, lower):
        predicted = jnp.dot(lower, weight, preferred_element_type=jnp.float32)
        mismatch = state - predicted
        weighted = (weighting * mismatch).astype(jnp.bfloat16)
        return mismatch, weighted

    for _ in range(ITERS):
        squashed, lowers = lower_inputs(states)
        new_states = []
        for state, q, lower in zip(states, squashed, lowers):
            mismatch, weighted = errors(state, lower)
            downward = lax.dot_general(
                weighted, weight, (((1,), (1,)), ((), ())), preferred_element_type=jnp.float32
            ).astype(jnp.bfloat16)
            from_above = shifted(downward, "layer", -1).astype(jnp.float32)
            descent = weighting * mismatch - (1.0 - q * q) * from_above
            new_states.append(jnp.where(clamped, state, state - step_rate * descent))
        states = new_states
    squashed, lowers = lower_inputs(states)
    weighteds = [errors(s, l)[1] for s, l in zip(states, lowers)]
    lower_input = jnp.concatenate(lowers, 0)
    weighted = jnp.concatenate(weighteds, 0)
    gradient = row_exchange_gradient(lower_input, weighted)[None]
    square_total = global_total(jnp.sum(gradient * gradient))
    entry_count = float(local_layers * layer_count * width * width)
    root_mean = jnp.sqrt(square_total / entry_count + 1e-06)
    clip_factor = jnp.minimum(1.0, 1.0 / root_mean)
    relaxed = jnp.concatenate(states, 0)[None]
    return (relaxed, (gradient * clip_factor).astype(jnp.bfloat16))


def solution(mesh):
    in_specs = (P("dp", None), P("layer", None, None), P("layer"), P("layer", "dp", None))
    out_specs = (P("layer", "dp", None), P("layer", "dp", None))
    return jax.shard_map(shards, mesh=mesh, in_specs=in_specs, out_specs=out_specs, check_vma=False)
```

```python
import jax
import jax.numpy as jnp
from jax import lax
from jax.sharding import PartitionSpec as P

ITERS = 5
CHUNKS = 2


step_rate = 0.1


def shifted(x, axis, by):
    length = lax.axis_size(axis)
    pairs = [(i, i + by) for i in range(length) if 0 <= i + by < length]
    return lax.ppermute(x, axis, pairs)


def row_exchange_gradient(lower_input, weighted):
    count = lax.axis_size("dp")
    index = lax.axis_index("dp")
    assert count == 4
    block = lower_input.shape[1] // count
    core = index % 2
    other_chip = 1 - index // 2

    def cols(a, start, size):
        return lax.dynamic_slice_in_dim(a, start, size, 1)

    across = jnp.concatenate([weighted, cols(lower_input, other_chip * 2 * block, 2 * block)], 1)
    arrived = lax.ppermute(across, "dp", [(j, j ^ 2) for j in range(count)])
    far_weighted = arrived[:, : weighted.shape[1]]
    far_columns = arrived[:, weighted.shape[1]:]
    partner = 1 - core
    beside = jnp.concatenate(
        [
            jnp.concatenate([weighted, cols(lower_input, (index ^ 1) * block, block)], 1),
            jnp.concatenate([far_weighted, cols(far_columns, partner * block, block)], 1),
        ],
        0,
    )
    near = lax.ppermute(beside, "dp", [(j, j ^ 1) for j in range(count)])
    own_rows = jnp.concatenate([cols(lower_input, index * block, block), cols(far_columns, core * block, block)], 0)
    own_weighted = jnp.concatenate([weighted, far_weighted], 0)
    total = jnp.einsum("rc,re->ce", own_rows, own_weighted, preferred_element_type=jnp.float32)
    total = total + jnp.einsum(
        "rc,re->ce", near[:, weighted.shape[1]:], near[:, : weighted.shape[1]], preferred_element_type=jnp.float32
    )
    return total


def global_total(value):
    axes = ("layer", "dp")
    count = lax.axis_size("layer") * lax.axis_size("dp")
    spread = jnp.broadcast_to(value, (count, 1))
    gathered = lax.all_to_all(spread, axes, 0, 0, tiled=True)
    return jnp.sum(gathered)


def shards(inputs, weights, precision, activity):
    layer_count = lax.axis_size("layer")
    position = lax.axis_index("layer")
    local_layers = weights.shape[0]
    assert local_layers == 1 and CHUNKS == 2
    width = weights.shape[1]
    weight = weights[0]
    weighting = precision[0]
    bottom_input = jnp.tanh(inputs.astype(jnp.float32)).astype(jnp.bfloat16)
    clamped = position == layer_count - 1
    rows = activity.shape[1]
    size = rows // CHUNKS
    states = [activity[0, c * size:(c + 1) * size] for c in range(CHUNKS)]
    bottoms = [bottom_input[c * size:(c + 1) * size] for c in range(CHUNKS)]

    def raised(q, c):
        arriving = shifted(q, "layer", 1)
        return jnp.where(position == 0, bottoms[c], arriving)

    def errors(state, lower):
        predicted = jnp.dot(lower, weight, preferred_element_type=jnp.float32)
        mismatch = state - predicted
        weighted = (weighting * mismatch).astype(jnp.bfloat16)
        return mismatch, weighted

    def carried_down(weighted):
        return lax.dot_general(
            weighted, weight, (((1,), (1,)), ((), ())), preferred_element_type=jnp.float32
        ).astype(jnp.bfloat16)

    def relaxed_step(state, q, mismatch, from_above):
        descent = weighting * mismatch - (1.0 - q * q) * from_above.astype(jnp.float32)
        return jnp.where(clamped, state, state - step_rate * descent)

    state_a, state_b = states
    q_a = jnp.tanh(state_a)
    lower_a = raised(q_a.astype(jnp.bfloat16), 0)
    q_b = jnp.tanh(state_b)
    for _ in range(ITERS):
        mismatch_a, weighted_a = errors(state_a, lower_a)
        down_a, up_b = lax.optimization_barrier((carried_down(weighted_a), q_b.astype(jnp.bfloat16)))
        above_a = shifted(down_a, "layer", -1)
        lower_b = raised(up_b, 1)
        mismatch_b, weighted_b = errors(state_b, lower_b)
        state_a = relaxed_step(state_a, q_a, mismatch_a, above_a)
        q_a = jnp.tanh(state_a)
        down_b, up_a = lax.optimization_barrier((carried_down(weighted_b), q_a.astype(jnp.bfloat16)))
        above_b = shifted(down_b, "layer", -1)
        lower_a = raised(up_a, 0)
        state_b = relaxed_step(state_b, q_b, mismatch_b, above_b)
        q_b = jnp.tanh(state_b)
    lower_b = raised(q_b.astype(jnp.bfloat16), 1)
    states = [state_a, state_b]
    lowers = [lower_a, lower_b]
    weighteds = [errors(s, l)[1] for s, l in zip(states, lowers)]
    lower_input = jnp.concatenate(lowers, 0)
    weighted = jnp.concatenate(weighteds, 0)
    gradient = row_exchange_gradient(lower_input, weighted)[None]
    square_total = global_total(jnp.sum(gradient * gradient))
    entry_count = float(local_layers * layer_count * width * width)
    root_mean = jnp.sqrt(square_total / entry_count + 1e-06)
    clip_factor = jnp.minimum(1.0, 1.0 / root_mean)
    relaxed = jnp.concatenate(states, 0)[None]
    return (relaxed, (gradient * clip_factor).astype(jnp.bfloat16))


def solution(mesh):
    in_specs = (P("dp", None), P("layer", None, None), P("layer"), P("layer", "dp", None))
    out_specs = (P("layer", "dp", None), P("layer", "dp", None))
    return jax.shard_map(shards, mesh=mesh, in_specs=in_specs, out_specs=out_specs, check_vma=False)
```

```python
import jax
import jax.numpy as jnp
from jax import lax
from jax.sharding import PartitionSpec as P

ITERS = 5
CHUNKS = 2


step_rate = 0.1


def shifted(x, axis, by):
    length = lax.axis_size(axis)
    pairs = [(i, (i + by) % length) for i in range(length)]
    return lax.ppermute(x, axis, pairs)


def row_exchange_gradient(lower_input, weighted):
    count = lax.axis_size("dp")
    index = lax.axis_index("dp")
    assert count == 4
    block = lower_input.shape[1] // count
    core = index % 2
    other_chip = 1 - index // 2

    def cols(a, start, size):
        return lax.dynamic_slice_in_dim(a, start, size, 1)

    across = jnp.concatenate([weighted, cols(lower_input, other_chip * 2 * block, 2 * block)], 1)
    arrived = lax.ppermute(across, "dp", [(j, j ^ 2) for j in range(count)])
    far_weighted = arrived[:, : weighted.shape[1]]
    far_columns = arrived[:, weighted.shape[1]:]
    partner = 1 - core
    beside = jnp.concatenate(
        [
            jnp.concatenate([weighted, cols(lower_input, (index ^ 1) * block, block)], 1),
            jnp.concatenate([far_weighted, cols(far_columns, partner * block, block)], 1),
        ],
        0,
    )
    near = lax.ppermute(beside, "dp", [(j, j ^ 1) for j in range(count)])
    own_rows = jnp.concatenate([cols(lower_input, index * block, block), cols(far_columns, core * block, block)], 0)
    own_weighted = jnp.concatenate([weighted, far_weighted], 0)
    total = jnp.einsum("rc,re->ce", own_rows, own_weighted, preferred_element_type=jnp.float32)
    total = total + jnp.einsum(
        "rc,re->ce", near[:, weighted.shape[1]:], near[:, : weighted.shape[1]], preferred_element_type=jnp.float32
    )
    return total


def global_total(value):
    axes = ("layer", "dp")
    count = lax.axis_size("layer") * lax.axis_size("dp")
    spread = jnp.broadcast_to(value, (count, 1))
    gathered = lax.all_to_all(spread, axes, 0, 0, tiled=True)
    return jnp.sum(gathered)


def shards(inputs, weights, precision, activity):
    layer_count = lax.axis_size("layer")
    position = lax.axis_index("layer")
    local_layers = weights.shape[0]
    assert local_layers == 1
    width = weights.shape[1]
    weight = weights[0]
    weighting = precision[0]
    bottom_input = jnp.tanh(inputs.astype(jnp.float32)).astype(jnp.bfloat16)
    clamped = position == layer_count - 1
    rows = activity.shape[1]
    size = rows // CHUNKS
    states = [activity[0, c * size:(c + 1) * size] for c in range(CHUNKS)]
    bottoms = [bottom_input[c * size:(c + 1) * size] for c in range(CHUNKS)]

    def lower_inputs(states):
        squashed = [jnp.tanh(s) for s in states]
        arriving = [shifted(q.astype(jnp.bfloat16), "layer", 1) for q in squashed]
        lowers = [jnp.where(position == 0, b, a) for b, a in zip(bottoms, arriving)]
        return squashed, lowers

    def errors(state, lower):
        predicted = jnp.dot(lower, weight, preferred_element_type=jnp.float32)
        mismatch = state - predicted
        weighted = (weighting * mismatch).astype(jnp.bfloat16)
        return mismatch, weighted

    for _ in range(ITERS):
        squashed, lowers = lower_inputs(states)
        new_states = []
        for state, q, lower in zip(states, squashed, lowers):
            mismatch, weighted = errors(state, lower)
            downward = lax.dot_general(
                weighted, weight, (((1,), (1,)), ((), ())), preferred_element_type=jnp.float32
            ).astype(jnp.bfloat16)
            from_above = shifted(downward, "layer", -1).astype(jnp.float32)
            from_above = jnp.where(clamped, 0.0, from_above)
            descent = weighting * mismatch - (1.0 - q * q) * from_above
            new_states.append(jnp.where(clamped, state, state - step_rate * descent))
        states = new_states
    squashed, lowers = lower_inputs(states)
    weighteds = [errors(s, l)[1] for s, l in zip(states, lowers)]
    lower_input = jnp.concatenate(lowers, 0)
    weighted = jnp.concatenate(weighteds, 0)
    gradient = row_exchange_gradient(lower_input, weighted)[None]
    square_total = global_total(jnp.sum(gradient * gradient))
    entry_count = float(local_layers * layer_count * width * width)
    root_mean = jnp.sqrt(square_total / entry_count + 1e-06)
    clip_factor = jnp.minimum(1.0, 1.0 / root_mean)
    relaxed = jnp.concatenate(states, 0)[None]
    return (relaxed, (gradient * clip_factor).astype(jnp.bfloat16))


def solution(mesh):
    in_specs = (P("dp", None), P("layer", None, None), P("layer"), P("layer", "dp", None))
    out_specs = (P("layer", "dp", None), P("layer", "dp", None))
    return jax.shard_map(shards, mesh=mesh, in_specs=in_specs, out_specs=out_specs, check_vma=False)
```

```python
import jax
import jax.numpy as jnp
from jax import lax
from jax.sharding import PartitionSpec as P

ITERS = 5
CHUNKS = 2


step_rate = 0.1


def shifted(x, axis, by):
    length = lax.axis_size(axis)
    pairs = [(i, (i + by) % length) for i in range(length)]
    return lax.ppermute(x, axis, pairs)


def row_exchange_gradient(lower_input, weighted):
    count = lax.axis_size("dp")
    index = lax.axis_index("dp")
    assert count == 4
    block = lower_input.shape[1] // count
    core = index % 2
    other_chip = 1 - index // 2

    def cols(a, start, size):
        return lax.dynamic_slice_in_dim(a, start, size, 1)

    across = jnp.concatenate([weighted, cols(lower_input, other_chip * 2 * block, 2 * block)], 1)
    arrived = lax.ppermute(across, "dp", [(j, j ^ 2) for j in range(count)])
    far_weighted = arrived[:, : weighted.shape[1]]
    far_columns = arrived[:, weighted.shape[1]:]
    partner = 1 - core
    beside = jnp.concatenate(
        [
            jnp.concatenate([weighted, cols(lower_input, (index ^ 1) * block, block)], 1),
            jnp.concatenate([far_weighted, cols(far_columns, partner * block, block)], 1),
        ],
        0,
    )
    near = lax.ppermute(beside, "dp", [(j, j ^ 1) for j in range(count)])
    own_rows = jnp.concatenate([cols(lower_input, index * block, block), cols(far_columns, core * block, block)], 0)
    own_weighted = jnp.concatenate([weighted, far_weighted], 0)
    total = jnp.einsum("rc,re->ce", own_rows, own_weighted, preferred_element_type=jnp.float32)
    total = total + jnp.einsum(
        "rc,re->ce", near[:, weighted.shape[1]:], near[:, : weighted.shape[1]], preferred_element_type=jnp.float32
    )
    return total


def global_total(value):
    axes = ("layer", "dp")
    count = lax.axis_size("layer") * lax.axis_size("dp")
    spread = jnp.broadcast_to(value, (count, 1))
    gathered = lax.all_to_all(spread, axes, 0, 0, tiled=True)
    return jnp.sum(gathered)


def shards(inputs, weights, precision, activity):
    layer_count = lax.axis_size("layer")
    position = lax.axis_index("layer")
    local_layers = weights.shape[0]
    assert local_layers == 1 and CHUNKS == 2
    width = weights.shape[1]
    weight = weights[0]
    weighting = precision[0]
    bottom_input = jnp.tanh(inputs.astype(jnp.float32)).astype(jnp.bfloat16)
    clamped = position == layer_count - 1
    rows = activity.shape[1]
    size = rows // CHUNKS
    states = [activity[0, c * size:(c + 1) * size] for c in range(CHUNKS)]
    bottoms = [bottom_input[c * size:(c + 1) * size] for c in range(CHUNKS)]

    def raised(q, c):
        arriving = shifted(q, "layer", 1)
        return jnp.where(position == 0, bottoms[c], arriving)

    def errors(state, lower):
        predicted = jnp.dot(lower, weight, preferred_element_type=jnp.float32)
        mismatch = state - predicted
        weighted = (weighting * mismatch).astype(jnp.bfloat16)
        return mismatch, weighted

    def carried_down(weighted):
        return lax.dot_general(
            weighted, weight, (((1,), (1,)), ((), ())), preferred_element_type=jnp.float32
        ).astype(jnp.bfloat16)

    def relaxed_step(state, q, mismatch, from_above):
        from_above = jnp.where(clamped, 0.0, from_above.astype(jnp.float32))
        descent = weighting * mismatch - (1.0 - q * q) * from_above
        return jnp.where(clamped, state, state - step_rate * descent)

    state_a, state_b = states
    q_a = jnp.tanh(state_a)
    lower_a = raised(q_a.astype(jnp.bfloat16), 0)
    q_b = jnp.tanh(state_b)
    for _ in range(ITERS):
        mismatch_a, weighted_a = errors(state_a, lower_a)
        down_a, up_b = lax.optimization_barrier((carried_down(weighted_a), q_b.astype(jnp.bfloat16)))
        above_a = shifted(down_a, "layer", -1)
        lower_b = raised(up_b, 1)
        mismatch_b, weighted_b = errors(state_b, lower_b)
        state_a = relaxed_step(state_a, q_a, mismatch_a, above_a)
        q_a = jnp.tanh(state_a)
        down_b, up_a = lax.optimization_barrier((carried_down(weighted_b), q_a.astype(jnp.bfloat16)))
        above_b = shifted(down_b, "layer", -1)
        lower_a = raised(up_a, 0)
        state_b = relaxed_step(state_b, q_b, mismatch_b, above_b)
        q_b = jnp.tanh(state_b)
    lower_b = raised(q_b.astype(jnp.bfloat16), 1)
    states = [state_a, state_b]
    lowers = [lower_a, lower_b]
    weighteds = [errors(s, l)[1] for s, l in zip(states, lowers)]
    lower_input = jnp.concatenate(lowers, 0)
    weighted = jnp.concatenate(weighteds, 0)
    gradient = row_exchange_gradient(lower_input, weighted)[None]
    square_total = global_total(jnp.sum(gradient * gradient))
    entry_count = float(local_layers * layer_count * width * width)
    root_mean = jnp.sqrt(square_total / entry_count + 1e-06)
    clip_factor = jnp.minimum(1.0, 1.0 / root_mean)
    relaxed = jnp.concatenate(states, 0)[None]
    return (relaxed, (gradient * clip_factor).astype(jnp.bfloat16))


def solution(mesh):
    in_specs = (P("dp", None), P("layer", None, None), P("layer"), P("layer", "dp", None))
    out_specs = (P("layer", "dp", None), P("layer", "dp", None))
    return jax.shard_map(shards, mesh=mesh, in_specs=in_specs, out_specs=out_specs, check_vma=False)
```

```python
import jax
import jax.numpy as jnp
from jax import lax
from jax.sharding import PartitionSpec as P

ITERS = 5
CHUNKS = 2


step_rate = 0.1


def shifted(x, axis, by):
    length = lax.axis_size(axis)
    pairs = [(i, (i + by) % length) for i in range(length)]
    return lax.ppermute(x, axis, pairs)


def row_exchange_gradient(lower_input, weighted):
    count = lax.axis_size("dp")
    index = lax.axis_index("dp")
    assert count == 4
    block = lower_input.shape[1] // count
    core = index % 2
    other_chip = 1 - index // 2

    def cols(a, start, size):
        return lax.dynamic_slice_in_dim(a, start, size, 1)

    across = jnp.concatenate([weighted, cols(lower_input, other_chip * 2 * block, 2 * block)], 1)
    arrived = lax.ppermute(across, "dp", [(j, j ^ 2) for j in range(count)])
    far_weighted = arrived[:, : weighted.shape[1]]
    far_columns = arrived[:, weighted.shape[1]:]
    partner = 1 - core
    beside = jnp.concatenate(
        [
            jnp.concatenate([weighted, cols(lower_input, (index ^ 1) * block, block)], 1),
            jnp.concatenate([far_weighted, cols(far_columns, partner * block, block)], 1),
        ],
        0,
    )
    near = lax.ppermute(beside, "dp", [(j, j ^ 1) for j in range(count)])
    own_rows = jnp.concatenate([cols(lower_input, index * block, block), cols(far_columns, core * block, block)], 0)
    own_weighted = jnp.concatenate([weighted, far_weighted], 0)
    total = jnp.einsum("rc,re->ce", own_rows, own_weighted, preferred_element_type=jnp.float32)
    total = total + jnp.einsum(
        "rc,re->ce", near[:, weighted.shape[1]:], near[:, : weighted.shape[1]], preferred_element_type=jnp.float32
    )
    return total


def global_total(value):
    axes = ("layer", "dp")
    count = lax.axis_size("layer") * lax.axis_size("dp")
    spread = jnp.broadcast_to(value, (count, 1))
    gathered = lax.all_to_all(spread, axes, 0, 0, tiled=True)
    return jnp.sum(gathered)


def shards(inputs, weights, precision, activity):
    layer_count = lax.axis_size("layer")
    position = lax.axis_index("layer")
    local_layers = weights.shape[0]
    assert local_layers == 1
    width = weights.shape[1]
    weight = weights[0]
    weight_t = lax.optimization_barrier(weight.T)
    weighting = precision[0]
    bottom_input = jnp.tanh(inputs.astype(jnp.float32)).astype(jnp.bfloat16)
    clamped = position == layer_count - 1
    rows = activity.shape[1]
    size = rows // CHUNKS
    states = [activity[0, c * size:(c + 1) * size] for c in range(CHUNKS)]
    bottoms = [bottom_input[c * size:(c + 1) * size] for c in range(CHUNKS)]

    def lower_inputs(states):
        squashed = [jnp.tanh(s) for s in states]
        arriving = [shifted(q.astype(jnp.bfloat16), "layer", 1) for q in squashed]
        lowers = [jnp.where(position == 0, b, a) for b, a in zip(bottoms, arriving)]
        return squashed, lowers

    def errors(state, lower):
        predicted = jnp.dot(lower, weight, preferred_element_type=jnp.float32)
        mismatch = state - predicted
        weighted = (weighting * mismatch).astype(jnp.bfloat16)
        return mismatch, weighted

    for _ in range(ITERS):
        squashed, lowers = lower_inputs(states)
        new_states = []
        for state, q, lower in zip(states, squashed, lowers):
            mismatch, weighted = errors(state, lower)
            downward = jnp.dot(weighted, weight_t, preferred_element_type=jnp.float32).astype(jnp.bfloat16)
            from_above = shifted(downward, "layer", -1).astype(jnp.float32)
            from_above = jnp.where(clamped, 0.0, from_above)
            descent = weighting * mismatch - (1.0 - q * q) * from_above
            new_states.append(jnp.where(clamped, state, state - step_rate * descent))
        states = new_states
    squashed, lowers = lower_inputs(states)
    weighteds = [errors(s, l)[1] for s, l in zip(states, lowers)]
    lower_input = jnp.concatenate(lowers, 0)
    weighted = jnp.concatenate(weighteds, 0)
    gradient = row_exchange_gradient(lower_input, weighted)[None]
    square_total = global_total(jnp.sum(gradient * gradient))
    entry_count = float(local_layers * layer_count * width * width)
    root_mean = jnp.sqrt(square_total / entry_count + 1e-06)
    clip_factor = jnp.minimum(1.0, 1.0 / root_mean)
    relaxed = jnp.concatenate(states, 0)[None]
    return (relaxed, (gradient * clip_factor).astype(jnp.bfloat16))


def solution(mesh):
    in_specs = (P("dp", None), P("layer", None, None), P("layer"), P("layer", "dp", None))
    out_specs = (P("layer", "dp", None), P("layer", "dp", None))
    return jax.shard_map(shards, mesh=mesh, in_specs=in_specs, out_specs=out_specs, check_vma=False)
```

```python
import jax
import jax.numpy as jnp
from jax import lax
from jax.sharding import PartitionSpec as P

ITERS = 5
CHUNKS = 2


step_rate = 0.1


def shifted(x, axis, by):
    length = lax.axis_size(axis)
    pairs = [(i, (i + by) % length) for i in range(length)]
    return lax.ppermute(x, axis, pairs)


def row_exchange_gradient(lowers, weighteds):
    count = lax.axis_size("dp")
    index = lax.axis_index("dp")
    assert count == 4
    block = lowers[0].shape[1] // count
    core = index % 2
    other_chip = 1 - index // 2

    def cols(a, start, size):
        return lax.dynamic_slice_in_dim(a, start, size, 1)

    arrived = []
    for lower, part in zip(lowers, weighteds):
        across = jnp.concatenate([part, cols(lower, other_chip * 2 * block, 2 * block)], 1)
        arrived.append(lax.ppermute(across, "dp", [(j, j ^ 2) for j in range(count)]))
    arrived = jnp.concatenate(arrived, 0)
    lower_input = jnp.concatenate(lowers, 0)
    weighted = jnp.concatenate(weighteds, 0)
    far_weighted = arrived[:, : weighted.shape[1]]
    far_columns = arrived[:, weighted.shape[1]:]
    partner = 1 - core
    beside = jnp.concatenate(
        [
            jnp.concatenate([weighted, cols(lower_input, (index ^ 1) * block, block)], 1),
            jnp.concatenate([far_weighted, cols(far_columns, partner * block, block)], 1),
        ],
        0,
    )
    near = lax.ppermute(beside, "dp", [(j, j ^ 1) for j in range(count)])
    own_rows = jnp.concatenate([cols(lower_input, index * block, block), cols(far_columns, core * block, block)], 0)
    own_weighted = jnp.concatenate([weighted, far_weighted], 0)
    total = jnp.einsum("rc,re->ce", own_rows, own_weighted, preferred_element_type=jnp.float32)
    total = total + jnp.einsum(
        "rc,re->ce", near[:, weighted.shape[1]:], near[:, : weighted.shape[1]], preferred_element_type=jnp.float32
    )
    return total


def global_total(value):
    axes = ("layer", "dp")
    count = lax.axis_size("layer") * lax.axis_size("dp")
    spread = jnp.broadcast_to(value, (count, 1))
    gathered = lax.all_to_all(spread, axes, 0, 0, tiled=True)
    return jnp.sum(gathered)


def shards(inputs, weights, precision, activity):
    layer_count = lax.axis_size("layer")
    position = lax.axis_index("layer")
    local_layers = weights.shape[0]
    assert local_layers == 1
    width = weights.shape[1]
    weight = weights[0]
    weighting = precision[0]
    bottom_input = jnp.tanh(inputs.astype(jnp.float32)).astype(jnp.bfloat16)
    clamped = position == layer_count - 1
    rows = activity.shape[1]
    size = rows // CHUNKS
    states = [activity[0, c * size:(c + 1) * size] for c in range(CHUNKS)]
    bottoms = [bottom_input[c * size:(c + 1) * size] for c in range(CHUNKS)]

    def lower_inputs(states):
        squashed = [jnp.tanh(s) for s in states]
        arriving = [shifted(q.astype(jnp.bfloat16), "layer", 1) for q in squashed]
        lowers = [jnp.where(position == 0, b, a) for b, a in zip(bottoms, arriving)]
        return squashed, lowers

    def errors(state, lower):
        predicted = jnp.dot(lower, weight, preferred_element_type=jnp.float32)
        mismatch = state - predicted
        weighted = (weighting * mismatch).astype(jnp.bfloat16)
        return mismatch, weighted

    for _ in range(ITERS):
        squashed, lowers = lower_inputs(states)
        new_states = []
        for state, q, lower in zip(states, squashed, lowers):
            mismatch, weighted = errors(state, lower)
            downward = lax.dot_general(
                weighted, weight, (((1,), (1,)), ((), ())), preferred_element_type=jnp.float32
            ).astype(jnp.bfloat16)
            from_above = shifted(downward, "layer", -1).astype(jnp.float32)
            from_above = jnp.where(clamped, 0.0, from_above)
            descent = weighting * mismatch - (1.0 - q * q) * from_above
            new_states.append(jnp.where(clamped, state, state - step_rate * descent))
        states = new_states
    squashed, lowers = lower_inputs(states)
    weighteds = [errors(s, l)[1] for s, l in zip(states, lowers)]
    gradient = row_exchange_gradient(lowers, weighteds)[None]
    square_total = global_total(jnp.sum(gradient * gradient))
    entry_count = float(local_layers * layer_count * width * width)
    root_mean = jnp.sqrt(square_total / entry_count + 1e-06)
    clip_factor = jnp.minimum(1.0, 1.0 / root_mean)
    relaxed = jnp.concatenate(states, 0)[None]
    return (relaxed, (gradient * clip_factor).astype(jnp.bfloat16))


def solution(mesh):
    in_specs = (P("dp", None), P("layer", None, None), P("layer"), P("layer", "dp", None))
    out_specs = (P("layer", "dp", None), P("layer", "dp", None))
    return jax.shard_map(shards, mesh=mesh, in_specs=in_specs, out_specs=out_specs, check_vma=False)
```

```python
import jax
import jax.numpy as jnp
from jax import lax
from jax.sharding import PartitionSpec as P

ITERS = 5
CHUNKS = 2


step_rate = 0.1


def shifted(x, axis, by):
    length = lax.axis_size(axis)
    pairs = [(i, (i + by) % length) for i in range(length)]
    return lax.ppermute(x, axis, pairs)


def row_exchange_gradient(lowers, weighteds):
    count = lax.axis_size("dp")
    index = lax.axis_index("dp")
    assert count == 4
    block = lowers[0].shape[1] // count
    core = index % 2
    other_chip = 1 - index // 2

    def cols(a, start, size):
        return lax.dynamic_slice_in_dim(a, start, size, 1)

    arrived = []
    for lower, part in zip(lowers, weighteds):
        across = jnp.concatenate([part, cols(lower, other_chip * 2 * block, 2 * block)], 1)
        arrived.append(lax.ppermute(across, "dp", [(j, j ^ 2) for j in range(count)]))
    arrived = jnp.concatenate(arrived, 0)
    lower_input = jnp.concatenate(lowers, 0)
    weighted = jnp.concatenate(weighteds, 0)
    far_weighted = arrived[:, : weighted.shape[1]]
    far_columns = arrived[:, weighted.shape[1]:]
    partner = 1 - core
    on_chip = [(j, j ^ 1) for j in range(count)]
    near_own = lax.ppermute(jnp.concatenate([weighted, cols(lower_input, (index ^ 1) * block, block)], 1), "dp", on_chip)
    near_far = lax.ppermute(jnp.concatenate([far_weighted, cols(far_columns, partner * block, block)], 1), "dp", on_chip)
    own_rows = jnp.concatenate([cols(lower_input, index * block, block), cols(far_columns, core * block, block)], 0)
    own_weighted = jnp.concatenate([weighted, far_weighted], 0)
    total = jnp.einsum("rc,re->ce", own_rows, own_weighted, preferred_element_type=jnp.float32)
    for near in (near_own, near_far):
        total = total + jnp.einsum(
            "rc,re->ce", near[:, weighted.shape[1]:], near[:, : weighted.shape[1]], preferred_element_type=jnp.float32
        )
    return total


def global_total(value):
    axes = ("layer", "dp")
    count = lax.axis_size("layer") * lax.axis_size("dp")
    spread = jnp.broadcast_to(value, (count, 1))
    gathered = lax.all_to_all(spread, axes, 0, 0, tiled=True)
    return jnp.sum(gathered)


def shards(inputs, weights, precision, activity):
    layer_count = lax.axis_size("layer")
    position = lax.axis_index("layer")
    local_layers = weights.shape[0]
    assert local_layers == 1
    width = weights.shape[1]
    weight = weights[0]
    weighting = precision[0]
    bottom_input = jnp.tanh(inputs.astype(jnp.float32)).astype(jnp.bfloat16)
    clamped = position == layer_count - 1
    rows = activity.shape[1]
    size = rows // CHUNKS
    states = [activity[0, c * size:(c + 1) * size] for c in range(CHUNKS)]
    bottoms = [bottom_input[c * size:(c + 1) * size] for c in range(CHUNKS)]

    def lower_inputs(states):
        squashed = [jnp.tanh(s) for s in states]
        arriving = [shifted(q.astype(jnp.bfloat16), "layer", 1) for q in squashed]
        lowers = [jnp.where(position == 0, b, a) for b, a in zip(bottoms, arriving)]
        return squashed, lowers

    def errors(state, lower):
        predicted = jnp.dot(lower, weight, preferred_element_type=jnp.float32)
        mismatch = state - predicted
        weighted = (weighting * mismatch).astype(jnp.bfloat16)
        return mismatch, weighted

    for _ in range(ITERS):
        squashed, lowers = lower_inputs(states)
        new_states = []
        for state, q, lower in zip(states, squashed, lowers):
            mismatch, weighted = errors(state, lower)
            downward = lax.dot_general(
                weighted, weight, (((1,), (1,)), ((), ())), preferred_element_type=jnp.float32
            ).astype(jnp.bfloat16)
            from_above = shifted(downward, "layer", -1).astype(jnp.float32)
            from_above = jnp.where(clamped, 0.0, from_above)
            descent = weighting * mismatch - (1.0 - q * q) * from_above
            new_states.append(jnp.where(clamped, state, state - step_rate * descent))
        states = new_states
    squashed, lowers = lower_inputs(states)
    weighteds = [errors(s, l)[1] for s, l in zip(states, lowers)]
    gradient = row_exchange_gradient(lowers, weighteds)[None]
    square_total = global_total(jnp.sum(gradient * gradient))
    entry_count = float(local_layers * layer_count * width * width)
    root_mean = jnp.sqrt(square_total / entry_count + 1e-06)
    clip_factor = jnp.minimum(1.0, 1.0 / root_mean)
    relaxed = jnp.concatenate(states, 0)[None]
    return (relaxed, (gradient * clip_factor).astype(jnp.bfloat16))


def solution(mesh):
    in_specs = (P("dp", None), P("layer", None, None), P("layer"), P("layer", "dp", None))
    out_specs = (P("layer", "dp", None), P("layer", "dp", None))
    return jax.shard_map(shards, mesh=mesh, in_specs=in_specs, out_specs=out_specs, check_vma=False)
```

```python
import jax
import jax.numpy as jnp
from jax import lax
from jax.sharding import PartitionSpec as P

ITERS = 5
CHUNKS = 4


step_rate = 0.1


def shifted(x, axis, by):
    length = lax.axis_size(axis)
    pairs = [(i, (i + by) % length) for i in range(length)]
    return lax.ppermute(x, axis, pairs)


def row_exchange_gradient(lowers, weighteds):
    count = lax.axis_size("dp")
    index = lax.axis_index("dp")
    assert count == 4
    block = lowers[0].shape[1] // count
    core = index % 2
    other_chip = 1 - index // 2

    def cols(a, start, size):
        return lax.dynamic_slice_in_dim(a, start, size, 1)

    arrived = []
    for lower, part in zip(lowers, weighteds):
        across = jnp.concatenate([part, cols(lower, other_chip * 2 * block, 2 * block)], 1)
        arrived.append(lax.ppermute(across, "dp", [(j, j ^ 2) for j in range(count)]))
    arrived = jnp.concatenate(arrived, 0)
    lower_input = jnp.concatenate(lowers, 0)
    weighted = jnp.concatenate(weighteds, 0)
    far_weighted = arrived[:, : weighted.shape[1]]
    far_columns = arrived[:, weighted.shape[1]:]
    partner = 1 - core
    on_chip = [(j, j ^ 1) for j in range(count)]
    near_own = lax.ppermute(jnp.concatenate([weighted, cols(lower_input, (index ^ 1) * block, block)], 1), "dp", on_chip)
    near_far = lax.ppermute(jnp.concatenate([far_weighted, cols(far_columns, partner * block, block)], 1), "dp", on_chip)
    own_rows = jnp.concatenate([cols(lower_input, index * block, block), cols(far_columns, core * block, block)], 0)
    own_weighted = jnp.concatenate([weighted, far_weighted], 0)
    total = jnp.einsum("rc,re->ce", own_rows, own_weighted, preferred_element_type=jnp.float32)
    for near in (near_own, near_far):
        total = total + jnp.einsum(
            "rc,re->ce", near[:, weighted.shape[1]:], near[:, : weighted.shape[1]], preferred_element_type=jnp.float32
        )
    return total


def global_total(value):
    axes = ("layer", "dp")
    count = lax.axis_size("layer") * lax.axis_size("dp")
    spread = jnp.broadcast_to(value, (count, 1))
    gathered = lax.all_to_all(spread, axes, 0, 0, tiled=True)
    return jnp.sum(gathered)


def shards(inputs, weights, precision, activity):
    layer_count = lax.axis_size("layer")
    position = lax.axis_index("layer")
    local_layers = weights.shape[0]
    assert local_layers == 1
    width = weights.shape[1]
    weight = weights[0]
    weighting = precision[0]
    bottom_input = jnp.tanh(inputs.astype(jnp.float32)).astype(jnp.bfloat16)
    clamped = position == layer_count - 1
    rows = activity.shape[1]
    size = rows // CHUNKS
    states = [activity[0, c * size:(c + 1) * size] for c in range(CHUNKS)]
    bottoms = [bottom_input[c * size:(c + 1) * size] for c in range(CHUNKS)]

    def lower_inputs(states):
        squashed = [jnp.tanh(s) for s in states]
        arriving = [shifted(q.astype(jnp.bfloat16), "layer", 1) for q in squashed]
        lowers = [jnp.where(position == 0, b, a) for b, a in zip(bottoms, arriving)]
        return squashed, lowers

    def errors(state, lower):
        predicted = jnp.dot(lower, weight, preferred_element_type=jnp.float32)
        mismatch = state - predicted
        weighted = (weighting * mismatch).astype(jnp.bfloat16)
        return mismatch, weighted

    for _ in range(ITERS):
        squashed, lowers = lower_inputs(states)
        new_states = []
        for state, q, lower in zip(states, squashed, lowers):
            mismatch, weighted = errors(state, lower)
            downward = lax.dot_general(
                weighted, weight, (((1,), (1,)), ((), ())), preferred_element_type=jnp.float32
            ).astype(jnp.bfloat16)
            from_above = shifted(downward, "layer", -1).astype(jnp.float32)
            from_above = jnp.where(clamped, 0.0, from_above)
            descent = weighting * mismatch - (1.0 - q * q) * from_above
            new_states.append(jnp.where(clamped, state, state - step_rate * descent))
        states = new_states
    squashed, lowers = lower_inputs(states)
    weighteds = [errors(s, l)[1] for s, l in zip(states, lowers)]
    gradient = row_exchange_gradient(lowers, weighteds)[None]
    square_total = global_total(jnp.sum(gradient * gradient))
    entry_count = float(local_layers * layer_count * width * width)
    root_mean = jnp.sqrt(square_total / entry_count + 1e-06)
    clip_factor = jnp.minimum(1.0, 1.0 / root_mean)
    relaxed = jnp.concatenate(states, 0)[None]
    return (relaxed, (gradient * clip_factor).astype(jnp.bfloat16))


def solution(mesh):
    in_specs = (P("dp", None), P("layer", None, None), P("layer"), P("layer", "dp", None))
    out_specs = (P("layer", "dp", None), P("layer", "dp", None))
    return jax.shard_map(shards, mesh=mesh, in_specs=in_specs, out_specs=out_specs, check_vma=False)
```

```python
import jax
import jax.numpy as jnp
from jax import lax
from jax.sharding import PartitionSpec as P

ITERS = 5
CHUNKS = 2


step_rate = 0.1


def shifted(x, axis, by):
    length = lax.axis_size(axis)
    pairs = [(i, (i + by) % length) for i in range(length)]
    return lax.ppermute(x, axis, pairs)


def row_exchange_gradient(lowers, weighteds):
    count = lax.axis_size("dp")
    index = lax.axis_index("dp")
    assert count == 4
    block = lowers[0].shape[1] // count
    core = index % 2
    other_chip = 1 - index // 2

    def cols(a, start, size):
        return lax.dynamic_slice_in_dim(a, start, size, 1)

    arrived = []
    for lower, part in zip(lowers, weighteds):
        across = jnp.concatenate([part, cols(lower, other_chip * 2 * block, 2 * block)], 1)
        arrived.append(lax.ppermute(across, "dp", [(j, j ^ 2) for j in range(count)]))
    arrived = jnp.concatenate(arrived, 0)
    lower_input = jnp.concatenate(lowers, 0)
    weighted = jnp.concatenate(weighteds, 0)
    far_weighted = arrived[:, : weighted.shape[1]]
    far_columns = arrived[:, weighted.shape[1]:]
    partner = 1 - core
    on_chip = [(j, j ^ 1) for j in range(count)]
    near_own = lax.ppermute(jnp.concatenate([weighted, cols(lower_input, (index ^ 1) * block, block)], 1), "dp", on_chip)
    near_far = lax.ppermute(jnp.concatenate([far_weighted, cols(far_columns, partner * block, block)], 1), "dp", on_chip)
    own_rows = jnp.concatenate([cols(lower_input, index * block, block), cols(far_columns, core * block, block)], 0)
    own_weighted = jnp.concatenate([weighted, far_weighted], 0)
    total = jnp.einsum("rc,re->ce", own_rows, own_weighted, preferred_element_type=jnp.float32)
    for near in (near_own, near_far):
        total = total + jnp.einsum(
            "rc,re->ce", near[:, weighted.shape[1]:], near[:, : weighted.shape[1]], preferred_element_type=jnp.float32
        )
    return total


def global_total(value):
    axes = ("dp", "layer")
    count = lax.axis_size("layer") * lax.axis_size("dp")
    spread = jnp.broadcast_to(value, (count, 1))
    gathered = lax.all_to_all(spread, axes, 0, 0, tiled=True)
    return jnp.sum(gathered)


def shards(inputs, weights, precision, activity):
    layer_count = lax.axis_size("layer")
    position = lax.axis_index("layer")
    local_layers = weights.shape[0]
    assert local_layers == 1
    width = weights.shape[1]
    weight = weights[0]
    weighting = precision[0]
    bottom_input = jnp.tanh(inputs.astype(jnp.float32)).astype(jnp.bfloat16)
    clamped = position == layer_count - 1
    rows = activity.shape[1]
    size = rows // CHUNKS
    states = [activity[0, c * size:(c + 1) * size] for c in range(CHUNKS)]
    bottoms = [bottom_input[c * size:(c + 1) * size] for c in range(CHUNKS)]

    def lower_inputs(states):
        squashed = [jnp.tanh(s) for s in states]
        arriving = [shifted(q.astype(jnp.bfloat16), "layer", 1) for q in squashed]
        lowers = [jnp.where(position == 0, b, a) for b, a in zip(bottoms, arriving)]
        return squashed, lowers

    def errors(state, lower):
        predicted = jnp.dot(lower, weight, preferred_element_type=jnp.float32)
        mismatch = state - predicted
        weighted = (weighting * mismatch).astype(jnp.bfloat16)
        return mismatch, weighted

    for _ in range(ITERS):
        squashed, lowers = lower_inputs(states)
        new_states = []
        for state, q, lower in zip(states, squashed, lowers):
            mismatch, weighted = errors(state, lower)
            downward = lax.dot_general(
                weighted, weight, (((1,), (1,)), ((), ())), preferred_element_type=jnp.float32
            ).astype(jnp.bfloat16)
            from_above = shifted(downward, "layer", -1).astype(jnp.float32)
            from_above = jnp.where(clamped, 0.0, from_above)
            descent = weighting * mismatch - (1.0 - q * q) * from_above
            new_states.append(jnp.where(clamped, state, state - step_rate * descent))
        states = new_states
    squashed, lowers = lower_inputs(states)
    weighteds = [errors(s, l)[1] for s, l in zip(states, lowers)]
    gradient = row_exchange_gradient(lowers, weighteds)[None]
    square_total = global_total(jnp.sum(gradient * gradient))
    entry_count = float(local_layers * layer_count * width * width)
    root_mean = jnp.sqrt(square_total / entry_count + 1e-06)
    clip_factor = jnp.minimum(1.0, 1.0 / root_mean)
    relaxed = jnp.concatenate(states, 0)[None]
    return (relaxed, (gradient * clip_factor).astype(jnp.bfloat16))


def solution(mesh):
    in_specs = (P("dp", None), P("layer", None, None), P("layer"), P("layer", "dp", None))
    out_specs = (P("layer", "dp", None), P("layer", "dp", None))
    return jax.shard_map(shards, mesh=mesh, in_specs=in_specs, out_specs=out_specs, check_vma=False)
```

```python
import jax
import jax.numpy as jnp
from jax import lax
from jax.sharding import PartitionSpec as P

ITERS = 5
CHUNKS = 2


step_rate = 0.1


def shifted(x, axis, by):
    length = lax.axis_size(axis)
    pairs = [(i, (i + by) % length) for i in range(length)]
    return lax.ppermute(x, axis, pairs)


def row_exchange_gradient(lowers, weighteds):
    count = lax.axis_size("dp")
    index = lax.axis_index("dp")
    assert count == 4
    block = lowers[0].shape[1] // count
    core = index % 2
    other_chip = 1 - index // 2

    def cols(a, start, size):
        return lax.dynamic_slice_in_dim(a, start, size, 1)

    on_chip = [(j, j ^ 1) for j in range(count)]
    width = weighteds[0].shape[1]
    partner = 1 - core
    far_weighted, far_columns, near_far = [], [], []
    for lower, part in zip(lowers, weighteds):
        across = jnp.concatenate([part, cols(lower, other_chip * 2 * block, 2 * block)], 1)
        arrived = lax.ppermute(across, "dp", [(j, j ^ 2) for j in range(count)])
        far_weighted.append(arrived[:, :width])
        far_columns.append(arrived[:, width:])
        forward = jnp.concatenate([arrived[:, :width], cols(arrived[:, width:], partner * block, block)], 1)
        near_far.append(lax.ppermute(forward, "dp", on_chip))
    lower_input = jnp.concatenate(lowers, 0)
    weighted = jnp.concatenate(weighteds, 0)
    far_weighted = jnp.concatenate(far_weighted, 0)
    far_columns = jnp.concatenate(far_columns, 0)
    near_own = lax.ppermute(jnp.concatenate([weighted, cols(lower_input, (index ^ 1) * block, block)], 1), "dp", on_chip)
    own_rows = jnp.concatenate([cols(lower_input, index * block, block), cols(far_columns, core * block, block)], 0)
    own_weighted = jnp.concatenate([weighted, far_weighted], 0)
    total = jnp.einsum("rc,re->ce", own_rows, own_weighted, preferred_element_type=jnp.float32)
    for near in [near_own] + near_far:
        total = total + jnp.einsum(
            "rc,re->ce", near[:, width:], near[:, :width], preferred_element_type=jnp.float32
        )
    return total


def global_total(value):
    axes = ("layer", "dp")
    count = lax.axis_size("layer") * lax.axis_size("dp")
    spread = jnp.broadcast_to(value, (count, 1))
    gathered = lax.all_to_all(spread, axes, 0, 0, tiled=True)
    return jnp.sum(gathered)


def shards(inputs, weights, precision, activity):
    layer_count = lax.axis_size("layer")
    position = lax.axis_index("layer")
    local_layers = weights.shape[0]
    assert local_layers == 1
    width = weights.shape[1]
    weight = weights[0]
    weighting = precision[0]
    bottom_input = jnp.tanh(inputs.astype(jnp.float32)).astype(jnp.bfloat16)
    clamped = position == layer_count - 1
    rows = activity.shape[1]
    size = rows // CHUNKS
    states = [activity[0, c * size:(c + 1) * size] for c in range(CHUNKS)]
    bottoms = [bottom_input[c * size:(c + 1) * size] for c in range(CHUNKS)]

    def lower_inputs(states):
        squashed = [jnp.tanh(s) for s in states]
        arriving = [shifted(q.astype(jnp.bfloat16), "layer", 1) for q in squashed]
        lowers = [jnp.where(position == 0, b, a) for b, a in zip(bottoms, arriving)]
        return squashed, lowers

    def errors(state, lower):
        predicted = jnp.dot(lower, weight, preferred_element_type=jnp.float32)
        mismatch = state - predicted
        weighted = (weighting * mismatch).astype(jnp.bfloat16)
        return mismatch, weighted

    for _ in range(ITERS):
        squashed, lowers = lower_inputs(states)
        new_states = []
        for state, q, lower in zip(states, squashed, lowers):
            mismatch, weighted = errors(state, lower)
            downward = lax.dot_general(
                weighted, weight, (((1,), (1,)), ((), ())), preferred_element_type=jnp.float32
            ).astype(jnp.bfloat16)
            from_above = shifted(downward, "layer", -1).astype(jnp.float32)
            from_above = jnp.where(clamped, 0.0, from_above)
            descent = weighting * mismatch - (1.0 - q * q) * from_above
            new_states.append(jnp.where(clamped, state, state - step_rate * descent))
        states = new_states
    squashed, lowers = lower_inputs(states)
    weighteds = [errors(s, l)[1] for s, l in zip(states, lowers)]
    gradient = row_exchange_gradient(lowers, weighteds)[None]
    square_total = global_total(jnp.sum(gradient * gradient))
    entry_count = float(local_layers * layer_count * width * width)
    root_mean = jnp.sqrt(square_total / entry_count + 1e-06)
    clip_factor = jnp.minimum(1.0, 1.0 / root_mean)
    relaxed = jnp.concatenate(states, 0)[None]
    return (relaxed, (gradient * clip_factor).astype(jnp.bfloat16))


def solution(mesh):
    in_specs = (P("dp", None), P("layer", None, None), P("layer"), P("layer", "dp", None))
    out_specs = (P("layer", "dp", None), P("layer", "dp", None))
    return jax.shard_map(shards, mesh=mesh, in_specs=in_specs, out_specs=out_specs, check_vma=False)
```

```python
import jax
import jax.numpy as jnp
from jax import lax
from jax.sharding import PartitionSpec as P

ITERS = 5
CHUNKS = 2


step_rate = 0.1


def shifted(x, axis, by):
    length = lax.axis_size(axis)
    pairs = [(i, (i + by) % length) for i in range(length)]
    return lax.ppermute(x, axis, pairs)


def row_exchange_gradient(lowers, weighteds):
    count = lax.axis_size("dp")
    index = lax.axis_index("dp")
    assert count == 4
    block = lowers[0].shape[1] // count
    core = index % 2
    other_chip = 1 - index // 2

    def cols(a, start, size):
        return lax.dynamic_slice_in_dim(a, start, size, 1)

    arrived = []
    for lower, part in zip(lowers, weighteds):
        across = jnp.concatenate([part, cols(lower, other_chip * 2 * block, 2 * block)], 1)
        arrived.append(lax.ppermute(across, "dp", [(j, j ^ 2) for j in range(count)]))
    arrived = jnp.concatenate(arrived, 0)
    lower_input = jnp.concatenate(lowers, 0)
    weighted = jnp.concatenate(weighteds, 0)
    far_weighted = arrived[:, : weighted.shape[1]]
    far_columns = arrived[:, weighted.shape[1]:]
    partner = 1 - core
    on_chip = [(j, j ^ 1) for j in range(count)]
    near_own = lax.ppermute(jnp.concatenate([weighted, cols(lower_input, (index ^ 1) * block, block)], 1), "dp", on_chip)
    near_far = lax.ppermute(jnp.concatenate([far_weighted, cols(far_columns, partner * block, block)], 1), "dp", on_chip)
    own_rows = jnp.concatenate([cols(lower_input, index * block, block), cols(far_columns, core * block, block)], 0)
    own_weighted = jnp.concatenate([weighted, far_weighted], 0)
    total = jnp.einsum("rc,re->ce", own_rows, own_weighted, preferred_element_type=jnp.float32)
    for near in (near_own, near_far):
        total = total + jnp.einsum(
            "rc,re->ce", near[:, weighted.shape[1]:], near[:, : weighted.shape[1]], preferred_element_type=jnp.float32
        )
    return total


def global_total(value):
    axes = ("layer", "dp")
    count = lax.axis_size("layer") * lax.axis_size("dp")
    spread = jnp.broadcast_to(value, (count, 1))
    gathered = lax.all_to_all(spread, axes, 0, 0, tiled=True)
    return jnp.sum(gathered)


def shards(inputs, weights, precision, activity):
    layer_count = lax.axis_size("layer")
    position = lax.axis_index("layer")
    local_layers = weights.shape[0]
    assert local_layers == 1
    width = weights.shape[1]
    weight = weights[0]
    weighting = precision[0]
    bottom_input = jnp.tanh(inputs.astype(jnp.float32)).astype(jnp.bfloat16)
    clamped = position == layer_count - 1
    rows = activity.shape[1]
    first = 3 * rows // 8
    bounds = [(0, first), (first, rows)]
    states = [activity[0, a:b] for a, b in bounds]
    bottoms = [bottom_input[a:b] for a, b in bounds]

    def lower_inputs(states):
        squashed = [jnp.tanh(s) for s in states]
        arriving = [shifted(q.astype(jnp.bfloat16), "layer", 1) for q in squashed]
        lowers = [jnp.where(position == 0, b, a) for b, a in zip(bottoms, arriving)]
        return squashed, lowers

    def errors(state, lower):
        predicted = jnp.dot(lower, weight, preferred_element_type=jnp.float32)
        mismatch = state - predicted
        weighted = (weighting * mismatch).astype(jnp.bfloat16)
        return mismatch, weighted

    for _ in range(ITERS):
        squashed, lowers = lower_inputs(states)
        new_states = []
        for state, q, lower in zip(states, squashed, lowers):
            mismatch, weighted = errors(state, lower)
            downward = lax.dot_general(
                weighted, weight, (((1,), (1,)), ((), ())), preferred_element_type=jnp.float32
            ).astype(jnp.bfloat16)
            from_above = shifted(downward, "layer", -1).astype(jnp.float32)
            from_above = jnp.where(clamped, 0.0, from_above)
            descent = weighting * mismatch - (1.0 - q * q) * from_above
            new_states.append(jnp.where(clamped, state, state - step_rate * descent))
        states = new_states
    squashed, lowers = lower_inputs(states)
    weighteds = [errors(s, l)[1] for s, l in zip(states, lowers)]
    gradient = row_exchange_gradient(lowers, weighteds)[None]
    square_total = global_total(jnp.sum(gradient * gradient))
    entry_count = float(local_layers * layer_count * width * width)
    root_mean = jnp.sqrt(square_total / entry_count + 1e-06)
    clip_factor = jnp.minimum(1.0, 1.0 / root_mean)
    relaxed = jnp.concatenate(states, 0)[None]
    return (relaxed, (gradient * clip_factor).astype(jnp.bfloat16))


def solution(mesh):
    in_specs = (P("dp", None), P("layer", None, None), P("layer"), P("layer", "dp", None))
    out_specs = (P("layer", "dp", None), P("layer", "dp", None))
    return jax.shard_map(shards, mesh=mesh, in_specs=in_specs, out_specs=out_specs, check_vma=False)
```

```python
import jax
import jax.numpy as jnp
from jax import lax
from jax.sharding import PartitionSpec as P

ITERS = 5
CHUNKS = 2


step_rate = 0.1


def shifted(x, axis, by):
    length = lax.axis_size(axis)
    pairs = [(i, (i + by) % length) for i in range(length)]
    return lax.ppermute(x, axis, pairs)


def row_exchange_gradient(lowers, weighteds):
    count = lax.axis_size("dp")
    index = lax.axis_index("dp")
    assert count == 4
    block = lowers[0].shape[1] // count
    core = index % 2
    other_chip = 1 - index // 2

    def cols(a, start, size):
        return lax.dynamic_slice_in_dim(a, start, size, 1)

    arrived = []
    for lower, part in zip(lowers, weighteds):
        across = jnp.concatenate([part, cols(lower, other_chip * 2 * block, 2 * block)], 1)
        arrived.append(lax.ppermute(across, "dp", [(j, j ^ 2) for j in range(count)]))
    arrived = jnp.concatenate(arrived, 0)
    lower_input = jnp.concatenate(lowers, 0)
    weighted = jnp.concatenate(weighteds, 0)
    far_weighted = arrived[:, : weighted.shape[1]]
    far_columns = arrived[:, weighted.shape[1]:]
    partner = 1 - core
    on_chip = [(j, j ^ 1) for j in range(count)]
    near_own = lax.ppermute(jnp.concatenate([weighted, cols(lower_input, (index ^ 1) * block, block)], 1), "dp", on_chip)
    near_far = lax.ppermute(jnp.concatenate([far_weighted, cols(far_columns, partner * block, block)], 1), "dp", on_chip)
    own_rows = jnp.concatenate([cols(lower_input, index * block, block), cols(far_columns, core * block, block)], 0)
    own_weighted = jnp.concatenate([weighted, far_weighted], 0)
    total = jnp.einsum("rc,re->ce", own_rows, own_weighted, preferred_element_type=jnp.float32)
    for near in (near_own, near_far):
        total = total + jnp.einsum(
            "rc,re->ce", near[:, weighted.shape[1]:], near[:, : weighted.shape[1]], preferred_element_type=jnp.float32
        )
    return total


def global_total(value):
    axes = ("layer", "dp")
    count = lax.axis_size("layer") * lax.axis_size("dp")
    spread = jnp.broadcast_to(value, (count, 1))
    gathered = lax.all_to_all(spread, axes, 0, 0, tiled=True)
    return jnp.sum(gathered)


def shards(inputs, weights, precision, activity):
    layer_count = lax.axis_size("layer")
    position = lax.axis_index("layer")
    local_layers = weights.shape[0]
    assert local_layers == 1
    width = weights.shape[1]
    weight = weights[0]
    weighting = precision[0]
    bottom_input = jnp.tanh(inputs.astype(jnp.float32)).astype(jnp.bfloat16)
    clamped = position == layer_count - 1
    rows = activity.shape[1]
    size = rows // CHUNKS
    states = [activity[0, c * size:(c + 1) * size] for c in range(CHUNKS)]
    bottoms = [bottom_input[c * size:(c + 1) * size] for c in range(CHUNKS)]

    def lower_inputs(states):
        squashed = [jnp.tanh(s) for s in states]
        arriving = [shifted(q.astype(jnp.bfloat16), "layer", 1) for q in squashed]
        lowers = [jnp.where(position == 0, b, a) for b, a in zip(bottoms, arriving)]
        return squashed, lowers

    def errors(state, lower):
        predicted = jnp.dot(lower, weight, preferred_element_type=jnp.float32)
        mismatch = state - predicted
        weighted = (weighting * mismatch).astype(jnp.bfloat16)
        return mismatch, weighted

    for _ in range(ITERS):
        squashed, lowers = lower_inputs(states)
        new_states = []
        for state, q, lower in zip(states, squashed, lowers):
            mismatch, weighted = errors(state, lower)
            downward = lax.dot_general(
                weighted, weight, (((1,), (1,)), ((), ())), preferred_element_type=jnp.float32
            ).astype(jnp.bfloat16)
            from_above = shifted(downward, "layer", -1).astype(jnp.float32)
            from_above = jnp.where(clamped, 0.0, from_above)
            descent = weighting * mismatch - (1.0 - q * q) * from_above
            new_states.append(jnp.where(clamped, state, state - step_rate * descent))
        states = new_states
    squashed, lowers = lower_inputs(states)
    weighteds = [errors(s, l)[1] for s, l in zip(states, lowers)]
    gradient = row_exchange_gradient(lowers, weighteds)[None]
    square_total = global_total(jnp.sum(lax.optimization_barrier(jnp.sum(gradient * gradient, axis=-1))))
    entry_count = float(local_layers * layer_count * width * width)
    root_mean = jnp.sqrt(square_total / entry_count + 1e-06)
    clip_factor = jnp.minimum(1.0, 1.0 / root_mean)
    relaxed = jnp.concatenate(states, 0)[None]
    return (relaxed, (gradient * clip_factor).astype(jnp.bfloat16))


def solution(mesh):
    in_specs = (P("dp", None), P("layer", None, None), P("layer"), P("layer", "dp", None))
    out_specs = (P("layer", "dp", None), P("layer", "dp", None))
    return jax.shard_map(shards, mesh=mesh, in_specs=in_specs, out_specs=out_specs, check_vma=False)
```

```python
import jax
import jax.numpy as jnp
from jax import lax
from jax.sharding import PartitionSpec as P

ITERS = 5
CHUNKS = 2


step_rate = 0.1


def shifted(x, axis, by):
    length = lax.axis_size(axis)
    pairs = [(i, (i + by) % length) for i in range(length)]
    return lax.ppermute(x, axis, pairs)


def row_exchange_gradient(lowers, weighteds):
    count = lax.axis_size("dp")
    index = lax.axis_index("dp")
    assert count == 4
    block = lowers[0].shape[1] // count
    core = index % 2
    other_chip = 1 - index // 2

    def cols(a, start, size):
        return lax.dynamic_slice_in_dim(a, start, size, 1)

    arrived = []
    for lower, part in zip(lowers, weighteds):
        across = jnp.concatenate([part, cols(lower, other_chip * 2 * block, 2 * block)], 1)
        arrived.append(lax.ppermute(across, "dp", [(j, j ^ 2) for j in range(count)]))
    arrived = jnp.concatenate(arrived, 0)
    lower_input = jnp.concatenate(lowers, 0)
    weighted = jnp.concatenate(weighteds, 0)
    far_weighted = arrived[:, : weighted.shape[1]]
    far_columns = arrived[:, weighted.shape[1]:]
    partner = 1 - core
    on_chip = [(j, j ^ 1) for j in range(count)]
    near_own = lax.ppermute(jnp.concatenate([weighted, cols(lower_input, (index ^ 1) * block, block)], 1), "dp", on_chip)
    near_far = lax.ppermute(jnp.concatenate([far_weighted, cols(far_columns, partner * block, block)], 1), "dp", on_chip)
    own_rows = jnp.concatenate([cols(lower_input, index * block, block), cols(far_columns, core * block, block)], 0)
    own_weighted = jnp.concatenate([weighted, far_weighted], 0)
    total = jnp.einsum("rc,re->ce", own_rows, own_weighted, preferred_element_type=jnp.float32)
    for near in (near_own, near_far):
        total = total + jnp.einsum(
            "rc,re->ce", near[:, weighted.shape[1]:], near[:, : weighted.shape[1]], preferred_element_type=jnp.float32
        )
    return total


def global_total(value):
    axes = ("layer", "dp")
    count = lax.axis_size("layer") * lax.axis_size("dp")
    spread = jnp.broadcast_to(value, (count, 1))
    gathered = lax.all_to_all(spread, axes, 0, 0, tiled=True)
    return jnp.sum(gathered)


def shards(inputs, weights, precision, activity):
    layer_count = lax.axis_size("layer")
    position = lax.axis_index("layer")
    local_layers = weights.shape[0]
    assert local_layers == 1
    width = weights.shape[1]
    weight = weights[0]
    weighting = precision[0]
    bottom_input = jnp.tanh(inputs.astype(jnp.float32)).astype(jnp.bfloat16)
    clamped = position == layer_count - 1
    rows = activity.shape[1]
    size = rows // CHUNKS
    states = [activity[0, c * size:(c + 1) * size] for c in range(CHUNKS)]
    bottoms = [bottom_input[c * size:(c + 1) * size] for c in range(CHUNKS)]

    def lower_inputs(states):
        squashed = [jnp.tanh(s) for s in states]
        arriving = [shifted(q.astype(jnp.bfloat16), "layer", 1) for q in squashed]
        lowers = [jnp.where(position == 0, b, a) for b, a in zip(bottoms, arriving)]
        return squashed, lowers

    def errors(state, lower):
        predicted = jnp.dot(lower, weight, preferred_element_type=jnp.float32)
        mismatch = state - predicted
        weighted = (weighting * mismatch).astype(jnp.bfloat16)
        return mismatch, weighted

    for _ in range(ITERS):
        squashed, lowers = lower_inputs(states)
        new_states = []
        for state, q, lower in zip(states, squashed, lowers):
            mismatch, weighted = errors(state, lower)
            downward = lax.dot_general(
                weighted, weight, (((1,), (1,)), ((), ())), preferred_element_type=jnp.float32
            ).astype(jnp.bfloat16)
            from_above = shifted(downward, "layer", -1).astype(jnp.float32)
            descent = weighting * mismatch - (1.0 - q * q) * from_above
            new_states.append(jnp.where(clamped, state, state - step_rate * descent))
        states = new_states
    squashed, lowers = lower_inputs(states)
    weighteds = [errors(s, l)[1] for s, l in zip(states, lowers)]
    gradient = row_exchange_gradient(lowers, weighteds)[None]
    square_total = global_total(jnp.sum(gradient * gradient))
    entry_count = float(local_layers * layer_count * width * width)
    root_mean = jnp.sqrt(square_total / entry_count + 1e-06)
    clip_factor = jnp.minimum(1.0, 1.0 / root_mean)
    relaxed = jnp.concatenate(states, 0)[None]
    return (relaxed, (gradient * clip_factor).astype(jnp.bfloat16))


def solution(mesh):
    in_specs = (P("dp", None), P("layer", None, None), P("layer"), P("layer", "dp", None))
    out_specs = (P("layer", "dp", None), P("layer", "dp", None))
    return jax.shard_map(shards, mesh=mesh, in_specs=in_specs, out_specs=out_specs, check_vma=False)
```
